512 devices in a mesh: segment: 4 (over x), seq: 16 (over y, z_hi), mp: 8 (over z_lo, core).
Axes of the slice: x: 4, y: 4, z: 16 (z_hi: 4, z_lo: 4; z = z_hi * 4 + z_lo), core: 2. Of those that a mesh axis runs over, the one named last changes fastest.
Arguments:
- sources: bfloat16 [4, 2048, 7168], P('segment', 'seq', 'mp'), may hold values from -6 to 6
- unite_weight: bfloat16 [4, 7168, 7168], P('segment', 'mp', 'seq'), may hold values from -4 to 4
- norm_gain: float32 [7168], P('seq'), may hold values from 0.5 to 1.5
- head_weight: bfloat16 [7168, 16000], P('seq', ('segment', 'mp')), may hold values from -6 to 6
- doc_lengths: int32 [12], replicated, may hold values from 1 to 512, 2048 in all
- target_ids: int32 [2048], P('seq'), may hold values from 0 to 19999
- teacher_ids: int32 [2048, 8], P('seq'), may hold values from 0 to 15999
- teacher_probs: float32 [2048, 8], P('seq'), may hold values from 0.001 to 0.5
Outputs:
- mean_loss: float32 [], replicated
- head_grad: float32 [7168, 16000], P('seq', ('segment', 'mp'))
The draws below stay inside these ranges and needn't reach their ends.
Inputs may be any that keep to these rules, and one draw needn't show every extreme that they name: `doc_lengths`: the longest document has exactly 512 tokens.
All inputs are finite; a program needn't handle non-finite values.
Results may differ from the reference program's by a relative error of at most 0.0042.
Values may be sent and summed in bfloat16 or wider, within the bound.
No kernel may reach another device: no remote copies, remote signals or barrier semaphores. Data moves between devices by JAX's collectives and lax.ppermute only.
A program may use at most 64 MiB of HBM per device.

```python
import math
import jax
import jax.numpy as jnp
import numpy as np
from jax import lax

D = 7168
VOCAB = 16000
SOURCES = 4
TOPK = 8
DOCS = 12
TOKENS = 2048
LONGEST = 512
N_MP = 8


def draw_head_weight(key, part):
    base = jax.random.normal(key, (D, VOCAB), jnp.float32) * D ** (-0.5)
    column_rise = 0.5 + 1.5 * jnp.arange(VOCAB, dtype=jnp.float32) / VOCAB
    base = base * column_rise[None, :]
    return jnp.clip(base, -6.0, 6.0).astype(jnp.bfloat16)


def draw_unite_weight(key, part):
    base = jax.random.normal(key, (SOURCES, D, D), jnp.float32) * (SOURCES * D) ** (-0.5)
    ramp = jnp.arange(D, dtype=jnp.float32) / D
    column_rise = jnp.exp(ramp * 2.3)
    shared = jax.random.normal(jax.random.fold_in(key, 7), (SOURCES, D, 1), jnp.float32) * (16.0 * (SOURCES * D) ** (-0.5))
    return jnp.clip(base * column_rise[None, None, :] + shared, -4.0, 4.0).astype(jnp.bfloat16)


def draw_teacher_probs(key, part):
    ramp = jnp.arange(TOKENS, dtype=jnp.float32) / TOKENS
    level = 0.01 + 0.4 * ramp
    spread = jax.random.uniform(key, (TOKENS, TOPK), jnp.float32, 0.5, 1.0)
    return jnp.clip(level[:, None] * spread, 0.001, 0.5)


def place_ends(values, stream_key, low, top_value):
    longest = values.shape.index(max(values.shape))
    spots = []
    for shift in (0, 1):
        where = [jax.random.randint(jax.random.fold_in(stream_key, axis), (), 0, length) for axis, length in enumerate(values.shape)]
        where[longest] = (where[longest] + shift) % values.shape[longest]
        spots.append(tuple(where))
    return values.at[spots[0]].set(low).at[spots[1]].set(top_value)


def level_of(own_key, extent, pieces, least, top_value):
    level = 1.0
    for position, shards_of in pieces:
        steps = jax.random.uniform(jax.random.fold_in(jax.random.fold_in(own_key, 6), position), (shards_of,), jnp.float32, least / len(pieces), top_value / len(pieces))
        level = level * jnp.repeat(jnp.exp(steps), extent[position] // shards_of).reshape((-1,) + (1,) * (len(extent) - 1 - position))
    return level


def rank_bounds(count, skew):
    weights = [(1 << 20) // math.isqrt(standing ** skew) + 1 for standing in range(1, count + 1)]
    scale = 1 + sum(weights) // (1 << 30)
    return np.cumsum(np.array([max(1, weight // scale) for weight in weights]))


def ranked_ids(stream_key, shape, amount, lean):
    grid = rank_bounds(amount, lean)
    ticket = jax.random.randint(jax.random.fold_in(stream_key, 1), shape, 0, int(grid[amount - 1]))
    standing = jnp.searchsorted(jnp.asarray(grid, jnp.int32), ticket, side="right")
    return jax.random.permutation(jax.random.fold_in(stream_key, 2), amount)[standing].astype(jnp.int32)


def split_up(amount, total, bound, lean):
    portions = [(1 << 20) // math.isqrt(standing ** lean) + 1 for standing in range(2, amount + 1)]
    spare, given = total - bound - (amount - 1), [1] * (amount - 1)
    while spare > 0:
        movable = [i for i in range(amount - 1) if given[i] < bound]
        whole, remaining = sum([portions[i] for i in movable]), spare
        for i in movable:
            more = min(bound - given[i], max(1, remaining * portions[i] // whole), spare)
            given[i] = given[i] + more
            spare = spare - more
    return np.array([bound] + given)


def ragged(stream_key, number_of, total, most, skew):
    if number_of == 2:
        one = jax.random.randint(stream_key, (), max(1, total - most), min(most, total - 1) + 1)
        return jnp.stack([one, total - one])
    tallies = jnp.asarray(split_up(number_of, total, most, skew), jnp.int32)
    twos = (number_of - 1) // 2
    source_of, taker = tallies[1:1 + 2 * twos:2], tallies[2:2 + 2 * twos:2]
    slack = jnp.minimum(source_of - 1, most - taker)
    passed = jax.random.randint(jax.random.fold_in(stream_key, 1), (twos,), 0, 1 << 20) % (slack + 1)
    tallies = tallies.at[1:1 + 2 * twos:2].set(source_of - passed).at[2:2 + 2 * twos:2].set(taker + passed)
    return tallies[jax.random.permutation(jax.random.fold_in(stream_key, 2), number_of)]


def noise(rng, shape, width, bound, cuts=(), kind=jnp.bfloat16):
    drawn = jax.random.normal(rng, shape, jnp.float32) * width
    if len(cuts) > 0:
        drawn = level_of(rng, shape, cuts, -0.22, 0.18) * drawn
    return jnp.clip(drawn, min=-bound, max=bound).astype(kind)


def setup_inputs(seed: int = 0) -> dict:
    arg_keys = jax.random.split(jax.random.key(seed), 9)
    return {
        "sources": noise(arg_keys[0], (SOURCES, TOKENS, D), 1.0, 6.0, ((0, 4), (1, 16), (2, 8))),
        "unite_weight": draw_unite_weight(jax.random.fold_in(arg_keys[8], 71), 0),
        "norm_gain": jnp.clip(1.0 + 0.1 * jax.random.normal(arg_keys[2], (D,), jnp.float32), 0.5, 1.5),
        "head_weight": draw_head_weight(jax.random.fold_in(arg_keys[8], 71), 0),
        "doc_lengths": ragged(arg_keys[4], DOCS, TOKENS, LONGEST, 0).astype(jnp.int32),
        "target_ids": place_ends(ranked_ids(arg_keys[5], (TOKENS,), VOCAB + VOCAB // 4, 1), jax.random.fold_in(arg_keys[5], 3), 0, (VOCAB + VOCAB // 4) - 1).astype(jnp.int32),
        "teacher_ids": place_ends(jax.random.randint(arg_keys[6], (TOKENS, TOPK), 0, VOCAB), jax.random.fold_in(arg_keys[6], 1), 0, VOCAB - 1).astype(jnp.int32),
        "teacher_probs": draw_teacher_probs(jax.random.fold_in(arg_keys[8], 71), 0),
    }


norm_eps = 1e-06

def reference(sources, unite_weight, norm_gain, head_weight, doc_lengths, target_ids, teacher_ids, teacher_probs):
    band = D // N_MP
    united = jnp.zeros((TOKENS, D), jnp.float32)
    for source in range(SOURCES):
        for block in range(N_MP):
            part = jnp.dot(sources[source][:, block * band:(block + 1) * band], unite_weight[source, block * band:(block + 1) * band, :], preferred_element_type=jnp.float32)
            rounded = lax.optimization_barrier(part.astype(jnp.bfloat16)).astype(jnp.float32)
            united = united + rounded
    mean_sq = lax.optimization_barrier(jnp.mean(united * united, axis=1, keepdims=True))
    hidden = (united * lax.rsqrt(mean_sq + norm_eps) * norm_gain[None, :]).astype(jnp.bfloat16)
    logits = jnp.dot(hidden, head_weight, preferred_element_type=jnp.float32)
    row_peak = lax.optimization_barrier(jnp.max(logits, axis=1))
    lse = row_peak + jnp.log(lax.optimization_barrier(jnp.sum(jnp.exp(logits - row_peak[:, None]), axis=1)))
    row_ids = jnp.arange(TOKENS, dtype=jnp.int32)
    in_vocab = (target_ids < VOCAB).astype(jnp.float32)
    safe_target = jnp.minimum(target_ids, VOCAB - 1).astype(jnp.int32)
    target_weight = jnp.zeros((TOKENS, VOCAB), jnp.float32)
    target_weight = target_weight.at[row_ids, safe_target].add(in_vocab)
    target_weight = target_weight.at[row_ids[:, None], teacher_ids].add(teacher_probs)
    picked = lax.optimization_barrier(jnp.sum(target_weight * logits, axis=1))
    target_mass = 1.0 + lax.optimization_barrier(jnp.sum(teacher_probs, axis=1))
    doc_ends = jnp.cumsum(doc_lengths).astype(jnp.int32)
    is_last = jnp.any(row_ids[:, None] + 1 == doc_ends[None, :], axis=1)
    valid_rows = jnp.where(is_last, 0.0, in_vocab).astype(jnp.float32)
    count = jnp.sum(valid_rows)
    mean_loss = jnp.sum(valid_rows * (target_mass * lse - picked)) / jnp.maximum(count, 1.0)
    logit_grad = (valid_rows[:, None] * (target_mass[:, None] * jnp.exp(logits - lse[:, None]) - target_weight)).astype(jnp.bfloat16)
    head_grad = lax.dot_general(hidden, logit_grad, (((0,), (0,)), ((), ())), preferred_element_type=jnp.float32)
    return (mean_loss, head_grad)
```

```python
import jax
import jax.numpy as jnp
from jax import lax
from jax.sharding import Mesh
from jax.sharding import PartitionSpec as P

D = 7168
VOCAB = 16000

norm_eps = 1e-06

SEQ = ("y", "zhi")
SM = ("segment", "zlo", "core")


def butterfly(value, axis, size, combine):
    step = 1
    while step < size:
        pairs = [(i, i ^ step) for i in range(size)]
        value = combine(value, lax.ppermute(value, axis, pairs))
        step *= 2
    return value


def add(a, b):
    return a + b


def merge_stats(a, b):
    peak = jnp.maximum(a[0], b[0])
    total = a[1] * jnp.exp(a[0] - peak) + b[1] * jnp.exp(b[0] - peak)
    return jnp.stack([peak, total, a[2] + b[2]])


def on_device(
    sources,
    unite_weight,
    norm_gain,
    head_weight,
    doc_lengths,
    target_ids,
    teacher_ids,
    teacher_probs,
    sizes,
):
    tok_local = sources.shape[1]
    n_sm = sizes["segment"] * sizes["zlo"] * sizes["core"]

    rows = lax.all_gather(sources[0], "zhi", axis=0, tiled=True)
    rows = lax.all_gather(rows, "y", axis=0, tiled=True)
    tokens = rows.shape[0]
    product = jnp.dot(rows, unite_weight[0], preferred_element_type=jnp.float32)
    product = lax.optimization_barrier(product.astype(jnp.bfloat16))

    pieces = lax.all_to_all(product, SM, 0, 0, tiled=True)
    slice_len = tokens // n_sm
    united = jnp.sum(
        pieces.reshape(n_sm, slice_len, -1).astype(jnp.float32), axis=0
    )

    squares = jnp.sum(united * united, axis=1)
    squares = butterfly(squares, "y", sizes["y"], add)
    squares = butterfly(squares, "zhi", sizes["zhi"], add)
    hidden_part = (
        united * lax.rsqrt(squares / D + norm_eps)[:, None] * norm_gain[None, :]
    ).astype(jnp.bfloat16)
    spread = jnp.broadcast_to(hidden_part[None], (n_sm,) + hidden_part.shape)
    hidden = lax.all_to_all(
        spread.reshape(tokens, -1), SM, 0, 0, tiled=True
    )

    logits = jnp.dot(hidden, head_weight, preferred_element_type=jnp.float32)
    logits = lax.psum_scatter(logits, "y", scatter_dimension=0, tiled=True)
    logits = lax.psum_scatter(logits, "zhi", scatter_dimension=0, tiled=True)

    seq_index = lax.axis_index("y") * sizes["zhi"] + lax.axis_index("zhi")
    positions = seq_index * tok_local + jnp.arange(tok_local, dtype=jnp.int32)
    vocab_width = head_weight.shape[1]
    offset = lax.axis_index(SM) * vocab_width
    columns = offset + jnp.arange(vocab_width, dtype=jnp.int32)
    target_weight = (target_ids[:, None] == columns[None, :]).astype(jnp.float32)
    for top_slot in range(teacher_ids.shape[1]):
        hits = (teacher_ids[:, top_slot : top_slot + 1] == columns[None, :]).astype(
            jnp.float32
        )
        target_weight = target_weight + teacher_probs[:, top_slot : top_slot + 1] * hits

    row_peak = jnp.max(logits, axis=1)
    stats = jnp.stack(
        [
            row_peak,
            jnp.sum(jnp.exp(logits - row_peak[:, None]), axis=1),
            jnp.sum(target_weight * logits, axis=1),
        ]
    )
    for axis in SM:
        stats = butterfly(stats, axis, sizes[axis], merge_stats)
    lse = stats[0] + jnp.log(stats[1])
    picked = stats[2]

    target_mass = 1.0 + jnp.sum(teacher_probs, axis=1)
    doc_ends = jnp.cumsum(doc_lengths)
    is_last = jnp.any(positions[:, None] + 1 == doc_ends[None, :], axis=1)
    in_vocab = (target_ids < VOCAB).astype(jnp.float32)
    valid_rows = jnp.where(is_last, 0.0, in_vocab)
    per_token = valid_rows * (target_mass * lse - picked)
    loss_hi = per_token.astype(jnp.bfloat16)
    loss_lo = (per_token - loss_hi.astype(jnp.float32)).astype(jnp.bfloat16)

    logit_grad = (
        valid_rows[:, None]
        * (target_mass[:, None] * jnp.exp(logits - lse[:, None]) - target_weight)
    ).astype(jnp.bfloat16)
    extra = jnp.stack(
        [loss_hi, loss_lo, valid_rows.astype(jnp.bfloat16), jnp.zeros_like(loss_hi)],
        axis=1,
    )
    carried = jnp.concatenate([logit_grad, extra], axis=1)
    carried = lax.all_gather(carried, "zhi", axis=0, tiled=True)
    carried = lax.all_gather(carried, "y", axis=0, tiled=True)

    loss_sum = jnp.sum(
        carried[:, vocab_width].astype(jnp.float32)
        + carried[:, vocab_width + 1].astype(jnp.float32)
    )
    count = jnp.sum(carried[:, vocab_width + 2].astype(jnp.float32))
    mean_loss = loss_sum / jnp.maximum(count, 1.0)

    head_grad = lax.dot_general(
        hidden,
        carried[:, :vocab_width],
        (((0,), (0,)), ((), ())),
        preferred_element_type=jnp.float32,
    )
    return (mean_loss, head_grad)


def solution(mesh):
    n_seg, n_seq, n_mp = (mesh.shape[a] for a in ("segment", "seq", "mp"))
    sizes = {"segment": n_seg, "y": n_seq // 4, "zhi": 4, "zlo": n_mp // 2, "core": 2}
    fine = Mesh(
        mesh.devices.reshape(n_seg, sizes["y"], sizes["zhi"], sizes["zlo"], sizes["core"]),
        ("segment", "y", "zhi", "zlo", "core"),
    )
    placed = (
        P("segment", SEQ, ("zlo", "core")),
        P("segment", ("zlo", "core"), SEQ),
        P(SEQ),
        P(SEQ, SM),
        P(),
        P(SEQ),
        P(SEQ, None),
        P(SEQ, None),
    )

    def body(*args):
        return on_device(*args, sizes=sizes)

    return jax.shard_map(
        body,
        mesh=fine,
        in_specs=placed,
        out_specs=(P(), P(SEQ, SM)),
        check_vma=False,
    )
```

```python
import jax
import jax.numpy as jnp
from jax import lax
from jax.sharding import Mesh
from jax.sharding import PartitionSpec as P

D = 7168
VOCAB = 16000

norm_eps = 1e-06

SEQ = ("y", "zhi")
SM = ("segment", "zlo", "core")


def gather_axis(value, axis, size):
    got = [value]
    for shift in range(1, size):
        pairs = [(i, (i + shift) % size) for i in range(size)]
        got.append(lax.ppermute(value, axis, pairs))
    rotated = jnp.stack([got[0]] + got[1:][::-1])
    me = lax.axis_index(axis)
    doubled = jnp.concatenate([rotated, rotated], axis=0)
    return lax.dynamic_slice_in_dim(doubled, (size - me) % size, size, axis=0)


def reduce_axis(value, axis, size, combine):
    every = gather_axis(value, axis, size)
    total = every[0]
    for k in range(1, size):
        total = combine(total, every[k])
    return total


def scatter_sum_axis(value, axis, size):
    me = lax.axis_index(axis)
    part = value.shape[0] // size
    total = lax.dynamic_slice_in_dim(value, me * part, part, axis=0)
    for shift in range(1, size):
        pairs = [(i, (i + shift) % size) for i in range(size)]
        chunk = lax.dynamic_slice_in_dim(value, ((me + shift) % size) * part, part, axis=0)
        total = total + lax.ppermute(chunk, axis, pairs)
    return total


def gather_rows_axis(value, axis, size):
    every = gather_axis(value, axis, size)
    return every.reshape((size * value.shape[0],) + value.shape[1:])


def add(a, b):
    return a + b


def merge_stats(a, b):
    peak = jnp.maximum(a[0], b[0])
    total = a[1] * jnp.exp(a[0] - peak) + b[1] * jnp.exp(b[0] - peak)
    return jnp.stack([peak, total, a[2] + b[2]])


def on_device(
    sources,
    unite_weight,
    norm_gain,
    head_weight,
    doc_lengths,
    target_ids,
    teacher_ids,
    teacher_probs,
    sizes,
):
    tok_local = sources.shape[1]
    n_sm = sizes["segment"] * sizes["zlo"] * sizes["core"]

    rows = gather_rows_axis(sources[0], "zhi", sizes["zhi"])
    rows = lax.all_gather(rows, "y", axis=0, tiled=True)
    tokens = rows.shape[0]
    product = jnp.dot(rows, unite_weight[0], preferred_element_type=jnp.float32)
    product = lax.optimization_barrier(product.astype(jnp.bfloat16))

    pieces = lax.all_to_all(product, SM, 0, 0, tiled=True)
    slice_len = tokens // n_sm
    united = jnp.sum(
        pieces.reshape(n_sm, slice_len, -1).astype(jnp.float32), axis=0
    )

    squares = jnp.sum(united * united, axis=1)
    squares = reduce_axis(squares, "y", sizes["y"], add)
    squares = reduce_axis(squares, "zhi", sizes["zhi"], add)
    hidden_part = (
        united * lax.rsqrt(squares / D + norm_eps)[:, None] * norm_gain[None, :]
    ).astype(jnp.bfloat16)
    spread = jnp.broadcast_to(hidden_part[None], (n_sm,) + hidden_part.shape)
    hidden = lax.all_to_all(
        spread.reshape(tokens, -1), SM, 0, 0, tiled=True
    )

    logits = jnp.dot(hidden, head_weight, preferred_element_type=jnp.float32)
    logits = lax.psum_scatter(logits, "y", scatter_dimension=0, tiled=True)
    logits = scatter_sum_axis(logits, "zhi", sizes["zhi"])

    seq_index = lax.axis_index("y") * sizes["zhi"] + lax.axis_index("zhi")
    positions = seq_index * tok_local + jnp.arange(tok_local, dtype=jnp.int32)
    vocab_width = head_weight.shape[1]
    offset = lax.axis_index(SM) * vocab_width
    columns = offset + jnp.arange(vocab_width, dtype=jnp.int32)
    target_weight = (target_ids[:, None] == columns[None, :]).astype(jnp.float32)
    for top_slot in range(teacher_ids.shape[1]):
        hits = (teacher_ids[:, top_slot : top_slot + 1] == columns[None, :]).astype(
            jnp.float32
        )
        target_weight = target_weight + teacher_probs[:, top_slot : top_slot + 1] * hits

    row_peak = jnp.max(logits, axis=1)
    stats = jnp.stack(
        [
            row_peak,
            jnp.sum(jnp.exp(logits - row_peak[:, None]), axis=1),
            jnp.sum(target_weight * logits, axis=1),
        ]
    )
    for axis in SM:
        stats = reduce_axis(stats, axis, sizes[axis], merge_stats)
    lse = stats[0] + jnp.log(stats[1])
    picked = stats[2]

    target_mass = 1.0 + jnp.sum(teacher_probs, axis=1)
    doc_ends = jnp.cumsum(doc_lengths)
    is_last = jnp.any(positions[:, None] + 1 == doc_ends[None, :], axis=1)
    in_vocab = (target_ids < VOCAB).astype(jnp.float32)
    valid_rows = jnp.where(is_last, 0.0, in_vocab)
    per_token = valid_rows * (target_mass * lse - picked)
    loss_hi = per_token.astype(jnp.bfloat16)
    loss_lo = (per_token - loss_hi.astype(jnp.float32)).astype(jnp.bfloat16)

    logit_grad = (
        valid_rows[:, None]
        * (target_mass[:, None] * jnp.exp(logits - lse[:, None]) - target_weight)
    ).astype(jnp.bfloat16)
    extra = jnp.stack(
        [loss_hi, loss_lo, valid_rows.astype(jnp.bfloat16), jnp.zeros_like(loss_hi)],
        axis=1,
    )
    carried = jnp.concatenate([logit_grad, extra], axis=1)
    carried = gather_rows_axis(carried, "zhi", sizes["zhi"])
    carried = lax.all_gather(carried, "y", axis=0, tiled=True)

    loss_sum = jnp.sum(
        carried[:, vocab_width].astype(jnp.float32)
        + carried[:, vocab_width + 1].astype(jnp.float32)
    )
    count = jnp.sum(carried[:, vocab_width + 2].astype(jnp.float32))
    mean_loss = loss_sum / jnp.maximum(count, 1.0)

    head_grad = lax.dot_general(
        hidden,
        carried[:, :vocab_width],
        (((0,), (0,)), ((), ())),
        preferred_element_type=jnp.float32,
    )
    return (mean_loss, head_grad)


def solution(mesh):
    n_seg, n_seq, n_mp = (mesh.shape[a] for a in ("segment", "seq", "mp"))
    sizes = {"segment": n_seg, "y": n_seq // 4, "zhi": 4, "zlo": n_mp // 2, "core": 2}
    fine = Mesh(
        mesh.devices.reshape(n_seg, sizes["y"], sizes["zhi"], sizes["zlo"], sizes["core"]),
        ("segment", "y", "zhi", "zlo", "core"),
    )
    placed = (
        P("segment", SEQ, ("zlo", "core")),
        P("segment", ("zlo", "core"), SEQ),
        P(SEQ),
        P(SEQ, SM),
        P(),
        P(SEQ),
        P(SEQ, None),
        P(SEQ, None),
    )

    def body(*args):
        return on_device(*args, sizes=sizes)

    return jax.shard_map(
        body,
        mesh=fine,
        in_specs=placed,
        out_specs=(P(), P(SEQ, SM)),
        check_vma=False,
    )
```

```python
import jax
import jax.numpy as jnp
from jax import lax
from jax.sharding import Mesh
from jax.sharding import PartitionSpec as P

D = 7168
VOCAB = 16000

norm_eps = 1e-06

SEQ = ("y", "zhi")
SM = ("segment", "zlo", "core")


def gather_axis(value, axis, size):
    got = [value]
    for shift in range(1, size):
        pairs = [(i, (i + shift) % size) for i in range(size)]
        got.append(lax.ppermute(value, axis, pairs))
    rotated = jnp.stack([got[0]] + got[1:][::-1])
    me = lax.axis_index(axis)
    doubled = jnp.concatenate([rotated, rotated], axis=0)
    return lax.dynamic_slice_in_dim(doubled, (size - me) % size, size, axis=0)


def reduce_axis(value, axis, size, combine):
    every = gather_axis(value, axis, size)
    total = every[0]
    for k in range(1, size):
        total = combine(total, every[k])
    return total


def scatter_sum_axis(value, axis, size):
    me = lax.axis_index(axis)
    part = value.shape[0] // size
    total = lax.dynamic_slice_in_dim(value, me * part, part, axis=0)
    for shift in range(1, size):
        pairs = [(i, (i + shift) % size) for i in range(size)]
        chunk = lax.dynamic_slice_in_dim(value, ((me + shift) % size) * part, part, axis=0)
        total = total + lax.ppermute(chunk, axis, pairs)
    return total


def gather_rows_axis(value, axis, size):
    every = gather_axis(value, axis, size)
    return every.reshape((size * value.shape[0],) + value.shape[1:])


def add(a, b):
    return a + b


def merge_stats(a, b):
    peak = jnp.maximum(a[0], b[0])
    total = a[1] * jnp.exp(a[0] - peak) + b[1] * jnp.exp(b[0] - peak)
    return jnp.stack([peak, total, a[2] + b[2]])


def half_pipeline(
    sources,
    unite_weight,
    norm_gain,
    head_weight,
    doc_lengths,
    target_ids,
    teacher_ids,
    teacher_probs,
    sizes,
    first,
    block,
):
    tok_local = sources.shape[1]
    n_sm = sizes["segment"] * sizes["zlo"] * sizes["core"]

    rows = gather_rows_axis(sources[0], "zhi", sizes["zhi"])
    rows = lax.all_gather(rows, "y", axis=0, tiled=True)
    tokens = rows.shape[0]
    product = jnp.dot(rows, unite_weight[0], preferred_element_type=jnp.float32)
    product = lax.optimization_barrier(product.astype(jnp.bfloat16))

    pieces = lax.all_to_all(product, SM, 0, 0, tiled=True)
    slice_len = tokens // n_sm
    united = jnp.sum(
        pieces.reshape(n_sm, slice_len, -1).astype(jnp.float32), axis=0
    )

    squares = jnp.sum(united * united, axis=1)
    squares = reduce_axis(squares, "y", sizes["y"], add)
    squares = reduce_axis(squares, "zhi", sizes["zhi"], add)
    hidden_part = (
        united * lax.rsqrt(squares / D + norm_eps)[:, None] * norm_gain[None, :]
    ).astype(jnp.bfloat16)
    spread = jnp.broadcast_to(hidden_part[None], (n_sm,) + hidden_part.shape)
    hidden = lax.all_to_all(
        spread.reshape(tokens, -1), SM, 0, 0, tiled=True
    )

    logits = jnp.dot(hidden, head_weight, preferred_element_type=jnp.float32)
    logits = lax.psum_scatter(logits, "y", scatter_dimension=0, tiled=True)
    logits = scatter_sum_axis(logits, "zhi", sizes["zhi"])

    seq_index = lax.axis_index("y") * sizes["zhi"] + lax.axis_index("zhi")
    positions = seq_index * block + first + jnp.arange(tok_local, dtype=jnp.int32)
    vocab_width = head_weight.shape[1]
    offset = lax.axis_index(SM) * vocab_width
    columns = offset + jnp.arange(vocab_width, dtype=jnp.int32)
    target_weight = (target_ids[:, None] == columns[None, :]).astype(jnp.float32)
    for top_slot in range(teacher_ids.shape[1]):
        hits = (teacher_ids[:, top_slot : top_slot + 1] == columns[None, :]).astype(
            jnp.float32
        )
        target_weight = target_weight + teacher_probs[:, top_slot : top_slot + 1] * hits

    row_peak = jnp.max(logits, axis=1)
    stats = jnp.stack(
        [
            row_peak,
            jnp.sum(jnp.exp(logits - row_peak[:, None]), axis=1),
            jnp.sum(target_weight * logits, axis=1),
        ]
    )
    for axis in SM:
        stats = reduce_axis(stats, axis, sizes[axis], merge_stats)
    lse = stats[0] + jnp.log(stats[1])
    picked = stats[2]

    target_mass = 1.0 + jnp.sum(teacher_probs, axis=1)
    doc_ends = jnp.cumsum(doc_lengths)
    is_last = jnp.any(positions[:, None] + 1 == doc_ends[None, :], axis=1)
    in_vocab = (target_ids < VOCAB).astype(jnp.float32)
    valid_rows = jnp.where(is_last, 0.0, in_vocab)
    per_token = valid_rows * (target_mass * lse - picked)
    loss_hi = per_token.astype(jnp.bfloat16)
    loss_lo = (per_token - loss_hi.astype(jnp.float32)).astype(jnp.bfloat16)

    logit_grad = (
        valid_rows[:, None]
        * (target_mass[:, None] * jnp.exp(logits - lse[:, None]) - target_weight)
    ).astype(jnp.bfloat16)
    extra = jnp.stack(
        [loss_hi, loss_lo, valid_rows.astype(jnp.bfloat16), jnp.zeros_like(loss_hi)],
        axis=1,
    )
    carried = jnp.concatenate([logit_grad, extra], axis=1)
    carried = gather_rows_axis(carried, "zhi", sizes["zhi"])
    carried = lax.all_gather(carried, "y", axis=0, tiled=True)

    loss_sum = jnp.sum(
        carried[:, vocab_width].astype(jnp.float32)
        + carried[:, vocab_width + 1].astype(jnp.float32)
    )
    count = jnp.sum(carried[:, vocab_width + 2].astype(jnp.float32))

    head_grad = lax.dot_general(
        hidden,
        carried[:, :vocab_width],
        (((0,), (0,)), ((), ())),
        preferred_element_type=jnp.float32,
    )
    return loss_sum, count, head_grad


def on_device(
    sources,
    unite_weight,
    norm_gain,
    head_weight,
    doc_lengths,
    target_ids,
    teacher_ids,
    teacher_probs,
    sizes,
    halves,
):
    block = sources.shape[1]
    width = block // halves
    loss_sum, count, head_grad = 0.0, 0.0, None
    for h in range(halves):
        cut = slice(h * width, (h + 1) * width)
        part_loss, part_count, part_grad = half_pipeline(
            sources[:, cut],
            unite_weight,
            norm_gain,
            head_weight,
            doc_lengths,
            target_ids[cut],
            teacher_ids[cut],
            teacher_probs[cut],
            sizes,
            h * width,
            block,
        )
        loss_sum = loss_sum + part_loss
        count = count + part_count
        head_grad = part_grad if head_grad is None else head_grad + part_grad
    mean_loss = loss_sum / jnp.maximum(count, 1.0)
    return (mean_loss, head_grad)


def solution(mesh):
    n_seg, n_seq, n_mp = (mesh.shape[a] for a in ("segment", "seq", "mp"))
    sizes = {"segment": n_seg, "y": n_seq // 4, "zhi": 4, "zlo": n_mp // 2, "core": 2}
    fine = Mesh(
        mesh.devices.reshape(n_seg, sizes["y"], sizes["zhi"], sizes["zlo"], sizes["core"]),
        ("segment", "y", "zhi", "zlo", "core"),
    )
    placed = (
        P("segment", SEQ, ("zlo", "core")),
        P("segment", ("zlo", "core"), SEQ),
        P(SEQ),
        P(SEQ, SM),
        P(),
        P(SEQ),
        P(SEQ, None),
        P(SEQ, None),
    )

    def body(*args):
        return on_device(*args, sizes=sizes, halves=2)

    return jax.shard_map(
        body,
        mesh=fine,
        in_specs=placed,
        out_specs=(P(), P(SEQ, SM)),
        check_vma=False,
    )
```

```python
import jax
import jax.numpy as jnp
from jax import lax
from jax.sharding import Mesh
from jax.sharding import PartitionSpec as P

D = 7168
VOCAB = 16000

norm_eps = 1e-06

SEQ = ("y", "zhi")
SM = ("segment", "zlo", "core")


def butterfly(value, axis, size, combine):
    step = 1
    while step < size:
        pairs = [(i, i ^ step) for i in range(size)]
        value = combine(value, lax.ppermute(value, axis, pairs))
        step *= 2
    return value


def add(a, b):
    return a + b


def merge_stats(a, b):
    peak = jnp.maximum(a[0], b[0])
    total = a[1] * jnp.exp(a[0] - peak) + b[1] * jnp.exp(b[0] - peak)
    return jnp.stack([peak, total, a[2] + b[2]])


def on_device(
    sources,
    unite_weight,
    norm_gain,
    head_weight,
    doc_lengths,
    target_ids,
    teacher_ids,
    teacher_probs,
    sizes,
):
    tok_local = sources.shape[1]
    n_sm = sizes["segment"] * sizes["zlo"] * sizes["core"]

    rows = lax.all_gather(sources[0], "zhi", axis=0, tiled=True)
    rows = lax.all_gather(rows, "y", axis=0, tiled=True)
    tokens = rows.shape[0]
    product = jnp.dot(rows, unite_weight[0], preferred_element_type=jnp.float32)
    product = lax.optimization_barrier(product.astype(jnp.bfloat16))

    n_sc = sizes["segment"] * sizes["core"]
    pieces = lax.all_to_all(product, ("segment", "core"), 0, 0, tiled=True)
    chunk = tokens // n_sc
    united = jnp.sum(pieces.reshape(n_sc, chunk, -1).astype(jnp.float32), axis=0)
    united = lax.psum_scatter(united, "zlo", scatter_dimension=0, tiled=True)

    squares = jnp.sum(united * united, axis=1)
    squares = lax.psum(squares, "y")
    squares = lax.psum(squares, "zhi")
    hidden_part = (
        united * lax.rsqrt(squares / D + norm_eps)[:, None] * norm_gain[None, :]
    ).astype(jnp.bfloat16)
    hidden_chunk = lax.all_gather(hidden_part, "zlo", axis=0, tiled=True)
    spread = jnp.broadcast_to(hidden_chunk[None], (n_sc,) + hidden_chunk.shape)
    hidden = lax.all_to_all(
        spread.reshape(tokens, -1), ("segment", "core"), 0, 0, tiled=True
    )

    logits = jnp.dot(hidden, head_weight, preferred_element_type=jnp.float32)
    logits = lax.psum_scatter(logits, "y", scatter_dimension=0, tiled=True)
    logits = lax.psum_scatter(logits, "zhi", scatter_dimension=0, tiled=True)

    seq_index = lax.axis_index("y") * sizes["zhi"] + lax.axis_index("zhi")
    positions = seq_index * tok_local + jnp.arange(tok_local, dtype=jnp.int32)
    vocab_width = head_weight.shape[1]
    offset = lax.axis_index(SM) * vocab_width
    columns = offset + jnp.arange(vocab_width, dtype=jnp.int32)
    target_weight = (target_ids[:, None] == columns[None, :]).astype(jnp.float32)
    for top_slot in range(teacher_ids.shape[1]):
        hits = (teacher_ids[:, top_slot : top_slot + 1] == columns[None, :]).astype(
            jnp.float32
        )
        target_weight = target_weight + teacher_probs[:, top_slot : top_slot + 1] * hits

    row_peak = jnp.max(logits, axis=1)
    stats = jnp.stack(
        [
            row_peak,
            jnp.sum(jnp.exp(logits - row_peak[:, None]), axis=1),
            jnp.sum(target_weight * logits, axis=1),
        ]
    )
    for axis in SM:
        stats = butterfly(stats, axis, sizes[axis], merge_stats)
    lse = stats[0] + jnp.log(stats[1])
    picked = stats[2]

    target_mass = 1.0 + jnp.sum(teacher_probs, axis=1)
    doc_ends = jnp.cumsum(doc_lengths)
    is_last = jnp.any(positions[:, None] + 1 == doc_ends[None, :], axis=1)
    in_vocab = (target_ids < VOCAB).astype(jnp.float32)
    valid_rows = jnp.where(is_last, 0.0, in_vocab)
    per_token = valid_rows * (target_mass * lse - picked)
    loss_hi = per_token.astype(jnp.bfloat16)
    loss_lo = (per_token - loss_hi.astype(jnp.float32)).astype(jnp.bfloat16)

    logit_grad = (
        valid_rows[:, None]
        * (target_mass[:, None] * jnp.exp(logits - lse[:, None]) - target_weight)
    ).astype(jnp.bfloat16)
    extra = jnp.stack(
        [loss_hi, loss_lo, valid_rows.astype(jnp.bfloat16), jnp.zeros_like(loss_hi)],
        axis=1,
    )
    carried = jnp.concatenate([logit_grad, extra], axis=1)
    carried = lax.all_gather(carried, "zhi", axis=0, tiled=True)
    carried = lax.all_gather(carried, "y", axis=0, tiled=True)

    loss_sum = jnp.sum(
        carried[:, vocab_width].astype(jnp.float32)
        + carried[:, vocab_width + 1].astype(jnp.float32)
    )
    count = jnp.sum(carried[:, vocab_width + 2].astype(jnp.float32))
    mean_loss = loss_sum / jnp.maximum(count, 1.0)

    head_grad = lax.dot_general(
        hidden,
        carried[:, :vocab_width],
        (((0,), (0,)), ((), ())),
        preferred_element_type=jnp.float32,
    )
    return (mean_loss, head_grad)


def solution(mesh):
    n_seg, n_seq, n_mp = (mesh.shape[a] for a in ("segment", "seq", "mp"))
    sizes = {"segment": n_seg, "y": n_seq // 4, "zhi": 4, "zlo": n_mp // 2, "core": 2}
    fine = Mesh(
        mesh.devices.reshape(n_seg, sizes["y"], sizes["zhi"], sizes["zlo"], sizes["core"]),
        ("segment", "y", "zhi", "zlo", "core"),
    )
    placed = (
        P("segment", SEQ, ("zlo", "core")),
        P("segment", ("zlo", "core"), SEQ),
        P(SEQ),
        P(SEQ, SM),
        P(),
        P(SEQ),
        P(SEQ, None),
        P(SEQ, None),
    )

    def body(*args):
        return on_device(*args, sizes=sizes)

    return jax.shard_map(
        body,
        mesh=fine,
        in_specs=placed,
        out_specs=(P(), P(SEQ, SM)),
        check_vma=False,
    )
```

```python
import jax
import jax.numpy as jnp
from jax import lax
from jax.sharding import Mesh
from jax.sharding import PartitionSpec as P

D = 7168
VOCAB = 16000

norm_eps = 1e-06

SEQ = ("y", "zhi")
SM = ("segment", "zlo", "core")


def spread_gather(value, axes, size):
    spread = jnp.broadcast_to(value[None], (size,) + value.shape)
    return lax.all_to_all(
        spread.reshape((size * value.shape[0],) + value.shape[1:]), axes, 0, 0, tiled=True
    )


def scatter_sum(value, axes, size):
    pieces = lax.all_to_all(value, axes, 0, 0, tiled=True)
    return jnp.sum(pieces.reshape((size, value.shape[0] // size) + value.shape[1:]), axis=0)


def on_device(
    sources,
    unite_weight,
    norm_gain,
    head_weight,
    doc_lengths,
    target_ids,
    teacher_ids,
    teacher_probs,
    sizes,
):
    tok_local = sources.shape[1]
    n_sm = sizes["segment"] * sizes["zlo"] * sizes["core"]

    rows = lax.all_gather(sources[0], "zhi", axis=0, tiled=True)
    rows = spread_gather(rows, "y", sizes["y"])
    tokens = rows.shape[0]
    product = jnp.dot(rows, unite_weight[0], preferred_element_type=jnp.float32)
    product = lax.optimization_barrier(product.astype(jnp.bfloat16))

    n_sc = sizes["segment"] * sizes["core"]
    pieces = lax.all_to_all(product, ("segment", "core"), 0, 0, tiled=True)
    chunk = tokens // n_sc
    united = jnp.sum(pieces.reshape(n_sc, chunk, -1).astype(jnp.float32), axis=0)
    united = scatter_sum(united, "zlo", sizes["zlo"])

    squares = jnp.sum(united * united, axis=1)
    squares = lax.psum(squares, "y")
    squares = lax.psum(squares, "zhi")
    hidden_part = (
        united * lax.rsqrt(squares / D + norm_eps)[:, None] * norm_gain[None, :]
    ).astype(jnp.bfloat16)
    hidden_chunk = lax.all_gather(hidden_part, "zlo", axis=0, tiled=True)
    spread = jnp.broadcast_to(hidden_chunk[None], (n_sc,) + hidden_chunk.shape)
    hidden = lax.all_to_all(
        spread.reshape(tokens, -1), ("segment", "core"), 0, 0, tiled=True
    )

    logits = jnp.dot(hidden, head_weight, preferred_element_type=jnp.float32)
    logits = lax.psum_scatter(logits, "y", scatter_dimension=0, tiled=True)
    logits = lax.psum_scatter(logits, "zhi", scatter_dimension=0, tiled=True)

    seq_index = lax.axis_index("y") * sizes["zhi"] + lax.axis_index("zhi")
    positions = seq_index * tok_local + jnp.arange(tok_local, dtype=jnp.int32)
    vocab_width = head_weight.shape[1]
    offset = lax.axis_index(SM) * vocab_width
    columns = offset + jnp.arange(vocab_width, dtype=jnp.int32)
    target_weight = (target_ids[:, None] == columns[None, :]).astype(jnp.float32)
    for top_slot in range(teacher_ids.shape[1]):
        hits = (teacher_ids[:, top_slot : top_slot + 1] == columns[None, :]).astype(
            jnp.float32
        )
        target_weight = target_weight + teacher_probs[:, top_slot : top_slot + 1] * hits

    row_peak = jnp.max(logits, axis=1)
    stats = jnp.stack(
        [
            row_peak,
            jnp.sum(jnp.exp(logits - row_peak[:, None]), axis=1),
            jnp.sum(target_weight * logits, axis=1),
        ]
    )
    n_sm = sizes["segment"] * sizes["zlo"] * sizes["core"]
    every = spread_gather(stats[None], SM, n_sm)
    peak = jnp.max(every[:, 0], axis=0)
    total = jnp.sum(every[:, 1] * jnp.exp(every[:, 0] - peak[None]), axis=0)
    lse = peak + jnp.log(total)
    picked = jnp.sum(every[:, 2], axis=0)

    target_mass = 1.0 + jnp.sum(teacher_probs, axis=1)
    doc_ends = jnp.cumsum(doc_lengths)
    is_last = jnp.any(positions[:, None] + 1 == doc_ends[None, :], axis=1)
    in_vocab = (target_ids < VOCAB).astype(jnp.float32)
    valid_rows = jnp.where(is_last, 0.0, in_vocab)
    per_token = valid_rows * (target_mass * lse - picked)
    loss_hi = per_token.astype(jnp.bfloat16)
    loss_lo = (per_token - loss_hi.astype(jnp.float32)).astype(jnp.bfloat16)

    logit_grad = (
        valid_rows[:, None]
        * (target_mass[:, None] * jnp.exp(logits - lse[:, None]) - target_weight)
    ).astype(jnp.bfloat16)
    extra = jnp.stack(
        [loss_hi, loss_lo, valid_rows.astype(jnp.bfloat16), jnp.zeros_like(loss_hi)],
        axis=1,
    )
    carried = jnp.concatenate([logit_grad, extra], axis=1)
    carried = lax.all_gather(carried, "zhi", axis=0, tiled=True)
    carried = spread_gather(carried, "y", sizes["y"])

    loss_sum = jnp.sum(
        carried[:, vocab_width].astype(jnp.float32)
        + carried[:, vocab_width + 1].astype(jnp.float32)
    )
    count = jnp.sum(carried[:, vocab_width + 2].astype(jnp.float32))
    mean_loss = loss_sum / jnp.maximum(count, 1.0)

    head_grad = lax.dot_general(
        hidden,
        carried[:, :vocab_width],
        (((0,), (0,)), ((), ())),
        preferred_element_type=jnp.float32,
    )
    return (mean_loss, head_grad)


def solution(mesh):
    n_seg, n_seq, n_mp = (mesh.shape[a] for a in ("segment", "seq", "mp"))
    sizes = {"segment": n_seg, "y": n_seq // 4, "zhi": 4, "zlo": n_mp // 2, "core": 2}
    fine = Mesh(
        mesh.devices.reshape(n_seg, sizes["y"], sizes["zhi"], sizes["zlo"], sizes["core"]),
        ("segment", "y", "zhi", "zlo", "core"),
    )
    placed = (
        P("segment", SEQ, ("zlo", "core")),
        P("segment", ("zlo", "core"), SEQ),
        P(SEQ),
        P(SEQ, SM),
        P(),
        P(SEQ),
        P(SEQ, None),
        P(SEQ, None),
    )

    def body(*args):
        return on_device(*args, sizes=sizes)

    return jax.shard_map(
        body,
        mesh=fine,
        in_specs=placed,
        out_specs=(P(), P(SEQ, SM)),
        check_vma=False,
    )
```

```python
import jax
import jax.numpy as jnp
from jax import lax
from jax.sharding import Mesh
from jax.sharding import PartitionSpec as P

D = 7168
VOCAB = 16000

norm_eps = 1e-06

SEQ = ("y", "zhi")
SM = ("segment", "zlo", "core")


def spread_gather(value, axes, size):
    spread = jnp.broadcast_to(value[None], (size,) + value.shape)
    return lax.all_to_all(
        spread.reshape((size * value.shape[0],) + value.shape[1:]), axes, 0, 0, tiled=True
    )


def scatter_sum(value, axes, size):
    pieces = lax.all_to_all(value, axes, 0, 0, tiled=True)
    return jnp.sum(pieces.reshape((size, value.shape[0] // size) + value.shape[1:]), axis=0)


def half_pipeline(sources, unite_weight, norm_gain, head_weight, sizes):
    n_sm = sizes["segment"] * sizes["zlo"] * sizes["core"]

    rows = lax.all_gather(sources[0], "zhi", axis=0, tiled=True)
    rows = spread_gather(rows, "y", sizes["y"])
    tokens = rows.shape[0]
    product = jnp.dot(rows, unite_weight[0], preferred_element_type=jnp.float32)
    product = lax.optimization_barrier(product.astype(jnp.bfloat16))

    n_sc = sizes["segment"] * sizes["core"]
    pieces = lax.all_to_all(product, ("segment", "core"), 0, 0, tiled=True)
    chunk = tokens // n_sc
    united = jnp.sum(pieces.reshape(n_sc, chunk, -1).astype(jnp.float32), axis=0)
    united = scatter_sum(united, "zlo", sizes["zlo"])

    squares = jnp.sum(united * united, axis=1)
    squares = lax.psum(squares, "y")
    squares = lax.psum(squares, "zhi")
    hidden_part = (
        united * lax.rsqrt(squares / D + norm_eps)[:, None] * norm_gain[None, :]
    ).astype(jnp.bfloat16)
    hidden_chunk = lax.all_gather(hidden_part, "zlo", axis=0, tiled=True)
    spread = jnp.broadcast_to(hidden_chunk[None], (n_sc,) + hidden_chunk.shape)
    hidden = lax.all_to_all(
        spread.reshape(tokens, -1), ("segment", "core"), 0, 0, tiled=True
    )

    logits = jnp.dot(hidden, head_weight, preferred_element_type=jnp.float32)
    return hidden, logits


def reduce_logits(logits):
    logits = lax.psum_scatter(logits, "y", scatter_dimension=0, tiled=True)
    return lax.psum_scatter(logits, "zhi", scatter_dimension=0, tiled=True)


def finish_half(
    hidden,
    logits,
    head_weight,
    doc_lengths,
    target_ids,
    teacher_ids,
    teacher_probs,
    sizes,
    first,
    block,
):
    tok_local = target_ids.shape[0]

    seq_index = lax.axis_index("y") * sizes["zhi"] + lax.axis_index("zhi")
    positions = seq_index * block + first + jnp.arange(tok_local, dtype=jnp.int32)
    vocab_width = head_weight.shape[1]
    offset = lax.axis_index(SM) * vocab_width
    columns = offset + jnp.arange(vocab_width, dtype=jnp.int32)
    target_weight = (target_ids[:, None] == columns[None, :]).astype(jnp.float32)
    for top_slot in range(teacher_ids.shape[1]):
        hits = (teacher_ids[:, top_slot : top_slot + 1] == columns[None, :]).astype(
            jnp.float32
        )
        target_weight = target_weight + teacher_probs[:, top_slot : top_slot + 1] * hits

    row_peak = jnp.max(logits, axis=1)
    stats = jnp.stack(
        [
            row_peak,
            jnp.sum(jnp.exp(logits - row_peak[:, None]), axis=1),
            jnp.sum(target_weight * logits, axis=1),
        ]
    )
    n_sm = sizes["segment"] * sizes["zlo"] * sizes["core"]
    every = spread_gather(stats[None], SM, n_sm)
    peak = jnp.max(every[:, 0], axis=0)
    total = jnp.sum(every[:, 1] * jnp.exp(every[:, 0] - peak[None]), axis=0)
    lse = peak + jnp.log(total)
    picked = jnp.sum(every[:, 2], axis=0)

    target_mass = 1.0 + jnp.sum(teacher_probs, axis=1)
    doc_ends = jnp.cumsum(doc_lengths)
    is_last = jnp.any(positions[:, None] + 1 == doc_ends[None, :], axis=1)
    in_vocab = (target_ids < VOCAB).astype(jnp.float32)
    valid_rows = jnp.where(is_last, 0.0, in_vocab)
    per_token = valid_rows * (target_mass * lse - picked)
    loss_hi = per_token.astype(jnp.bfloat16)
    loss_lo = (per_token - loss_hi.astype(jnp.float32)).astype(jnp.bfloat16)

    logit_grad = (
        valid_rows[:, None]
        * (target_mass[:, None] * jnp.exp(logits - lse[:, None]) - target_weight)
    ).astype(jnp.bfloat16)
    extra = jnp.stack(
        [loss_hi, loss_lo, valid_rows.astype(jnp.bfloat16), jnp.zeros_like(loss_hi)],
        axis=1,
    )
    carried = jnp.concatenate([logit_grad, extra], axis=1)
    carried = lax.all_gather(carried, "zhi", axis=0, tiled=True)
    carried = spread_gather(carried, "y", sizes["y"])

    loss_sum = jnp.sum(
        carried[:, vocab_width].astype(jnp.float32)
        + carried[:, vocab_width + 1].astype(jnp.float32)
    )
    count = jnp.sum(carried[:, vocab_width + 2].astype(jnp.float32))

    head_grad = lax.dot_general(
        hidden,
        carried[:, :vocab_width],
        (((0,), (0,)), ((), ())),
        preferred_element_type=jnp.float32,
    )
    return loss_sum, count, head_grad


def on_device(
    sources,
    unite_weight,
    norm_gain,
    head_weight,
    doc_lengths,
    target_ids,
    teacher_ids,
    teacher_probs,
    sizes,
    halves,
):
    block = sources.shape[1]
    width = block // halves
    cuts = [slice(h * width, (h + 1) * width) for h in range(halves)]
    fronts, reduced = [], []
    gate = None
    for h, cut in enumerate(cuts):
        part = sources[:, cut]
        if gate is not None:
            part = lax.optimization_barrier((part, gate))[0]
        hidden, logits = half_pipeline(part, unite_weight, norm_gain, head_weight, sizes)
        fronts.append(hidden)
        reduced.append(reduce_logits(logits))
        gate = logits
    loss_sum, count, head_grad = 0.0, 0.0, None
    for h, cut in enumerate(cuts):
        logits = reduced[h]
        if h + 1 < halves:
            logits = lax.optimization_barrier((logits, fronts[h + 1]))[0]
        part_loss, part_count, part_grad = finish_half(
            fronts[h],
            logits,
            head_weight,
            doc_lengths,
            target_ids[cut],
            teacher_ids[cut],
            teacher_probs[cut],
            sizes,
            h * width,
            block,
        )
        loss_sum = loss_sum + part_loss
        count = count + part_count
        head_grad = part_grad if head_grad is None else head_grad + part_grad
    mean_loss = loss_sum / jnp.maximum(count, 1.0)
    return (mean_loss, head_grad)


def solution(mesh):
    n_seg, n_seq, n_mp = (mesh.shape[a] for a in ("segment", "seq", "mp"))
    sizes = {"segment": n_seg, "y": n_seq // 4, "zhi": 4, "zlo": n_mp // 2, "core": 2}
    fine = Mesh(
        mesh.devices.reshape(n_seg, sizes["y"], sizes["zhi"], sizes["zlo"], sizes["core"]),
        ("segment", "y", "zhi", "zlo", "core"),
    )
    placed = (
        P("segment", SEQ, ("zlo", "core")),
        P("segment", ("zlo", "core"), SEQ),
        P(SEQ),
        P(SEQ, SM),
        P(),
        P(SEQ),
        P(SEQ, None),
        P(SEQ, None),
    )

    def body(*args):
        return on_device(*args, sizes=sizes, halves=2)

    return jax.shard_map(
        body,
        mesh=fine,
        in_specs=placed,
        out_specs=(P(), P(SEQ, SM)),
        check_vma=False,
    )
```

```python
import jax
import jax.numpy as jnp
from jax import lax
from jax.sharding import Mesh
from jax.sharding import PartitionSpec as P

D = 7168
VOCAB = 16000

norm_eps = 1e-06

SEQ = ("y", "zhi")
SM = ("segment", "zlo", "core")


def spread_gather(value, axes, size):
    spread = jnp.broadcast_to(value[None], (size,) + value.shape)
    return lax.all_to_all(
        spread.reshape((size * value.shape[0],) + value.shape[1:]), axes, 0, 0, tiled=True
    )


def scatter_sum(value, axes, size):
    pieces = lax.all_to_all(value, axes, 0, 0, tiled=True)
    return jnp.sum(pieces.reshape((size, value.shape[0] // size) + value.shape[1:]), axis=0)


def on_device(
    sources,
    unite_weight,
    norm_gain,
    head_weight,
    doc_lengths,
    target_ids,
    teacher_ids,
    teacher_probs,
    sizes,
):
    tok_local = sources.shape[1]
    n_sm = sizes["segment"] * sizes["zlo"] * sizes["core"]

    rows = lax.all_gather(sources[0], "zhi", axis=0, tiled=True)
    rows = spread_gather(rows, "y", sizes["y"])
    tokens = rows.shape[0]
    product = jnp.dot(rows, unite_weight[0], preferred_element_type=jnp.float32)
    product = lax.optimization_barrier(product.astype(jnp.bfloat16))

    n_sc = sizes["segment"] * sizes["core"]
    pieces = lax.all_to_all(product, ("segment", "core"), 0, 0, tiled=True)
    chunk = tokens // n_sc
    united = jnp.sum(pieces.reshape(n_sc, chunk, -1).astype(jnp.float32), axis=0)
    united = scatter_sum(united, "zlo", sizes["zlo"])

    squares = jnp.sum(united * united, axis=1)
    n_seq = sizes["y"] * sizes["zhi"]
    squares = jnp.sum(spread_gather(squares[None], SEQ, n_seq), axis=0)
    hidden_part = (
        united * lax.rsqrt(squares / D + norm_eps)[:, None] * norm_gain[None, :]
    ).astype(jnp.bfloat16)
    hidden_chunk = lax.all_gather(hidden_part, "zlo", axis=0, tiled=True)
    spread = jnp.broadcast_to(hidden_chunk[None], (n_sc,) + hidden_chunk.shape)
    hidden = lax.all_to_all(
        spread.reshape(tokens, -1), ("segment", "core"), 0, 0, tiled=True
    )

    logits = jnp.dot(hidden, head_weight, preferred_element_type=jnp.float32)
    logits = scatter_sum(logits, "y", sizes["y"])
    logits = scatter_sum(logits, "zhi", sizes["zhi"])

    seq_index = lax.axis_index("y") * sizes["zhi"] + lax.axis_index("zhi")
    positions = seq_index * tok_local + jnp.arange(tok_local, dtype=jnp.int32)
    vocab_width = head_weight.shape[1]
    offset = lax.axis_index(SM) * vocab_width
    columns = offset + jnp.arange(vocab_width, dtype=jnp.int32)
    target_weight = (target_ids[:, None] == columns[None, :]).astype(jnp.float32)
    for top_slot in range(teacher_ids.shape[1]):
        hits = (teacher_ids[:, top_slot : top_slot + 1] == columns[None, :]).astype(
            jnp.float32
        )
        target_weight = target_weight + teacher_probs[:, top_slot : top_slot + 1] * hits

    row_peak = jnp.max(logits, axis=1)
    stats = jnp.stack(
        [
            row_peak,
            jnp.sum(jnp.exp(logits - row_peak[:, None]), axis=1),
            jnp.sum(target_weight * logits, axis=1),
        ]
    )
    n_sm = sizes["segment"] * sizes["zlo"] * sizes["core"]
    every = spread_gather(stats[None], SM, n_sm)
    peak = jnp.max(every[:, 0], axis=0)
    total = jnp.sum(every[:, 1] * jnp.exp(every[:, 0] - peak[None]), axis=0)
    lse = peak + jnp.log(total)
    picked = jnp.sum(every[:, 2], axis=0)

    target_mass = 1.0 + jnp.sum(teacher_probs, axis=1)
    doc_ends = jnp.cumsum(doc_lengths)
    is_last = jnp.any(positions[:, None] + 1 == doc_ends[None, :], axis=1)
    in_vocab = (target_ids < VOCAB).astype(jnp.float32)
    valid_rows = jnp.where(is_last, 0.0, in_vocab)
    per_token = valid_rows * (target_mass * lse - picked)
    loss_hi = per_token.astype(jnp.bfloat16)
    loss_lo = (per_token - loss_hi.astype(jnp.float32)).astype(jnp.bfloat16)

    logit_grad = (
        valid_rows[:, None]
        * (target_mass[:, None] * jnp.exp(logits - lse[:, None]) - target_weight)
    ).astype(jnp.bfloat16)
    extra = jnp.stack(
        [loss_hi, loss_lo, valid_rows.astype(jnp.bfloat16), jnp.zeros_like(loss_hi)],
        axis=1,
    )
    carried = jnp.concatenate([logit_grad, extra], axis=1)
    carried = lax.all_gather(carried, "zhi", axis=0, tiled=True)
    carried = spread_gather(carried, "y", sizes["y"])

    loss_sum = jnp.sum(
        carried[:, vocab_width].astype(jnp.float32)
        + carried[:, vocab_width + 1].astype(jnp.float32)
    )
    count = jnp.sum(carried[:, vocab_width + 2].astype(jnp.float32))
    mean_loss = loss_sum / jnp.maximum(count, 1.0)

    head_grad = lax.dot_general(
        hidden,
        carried[:, :vocab_width],
        (((0,), (0,)), ((), ())),
        preferred_element_type=jnp.float32,
    )
    return (mean_loss, head_grad)


def solution(mesh):
    n_seg, n_seq, n_mp = (mesh.shape[a] for a in ("segment", "seq", "mp"))
    sizes = {"segment": n_seg, "y": n_seq // 4, "zhi": 4, "zlo": n_mp // 2, "core": 2}
    fine = Mesh(
        mesh.devices.reshape(n_seg, sizes["y"], sizes["zhi"], sizes["zlo"], sizes["core"]),
        ("segment", "y", "zhi", "zlo", "core"),
    )
    placed = (
        P("segment", SEQ, ("zlo", "core")),
        P("segment", ("zlo", "core"), SEQ),
        P(SEQ),
        P(SEQ, SM),
        P(),
        P(SEQ),
        P(SEQ, None),
        P(SEQ, None),
    )

    def body(*args):
        return on_device(*args, sizes=sizes)

    return jax.shard_map(
        body,
        mesh=fine,
        in_specs=placed,
        out_specs=(P(), P(SEQ, SM)),
        check_vma=False,
    )
```

```python
import jax
import jax.numpy as jnp
from jax import lax
from jax.sharding import Mesh
from jax.sharding import PartitionSpec as P

D = 7168
VOCAB = 16000

norm_eps = 1e-06

SEQ = ("y", "zhi")
SM = ("segment", "zlo", "core")


def spread_gather(value, axes, size):
    spread = jnp.broadcast_to(value[None], (size,) + value.shape)
    return lax.all_to_all(
        spread.reshape((size * value.shape[0],) + value.shape[1:]), axes, 0, 0, tiled=True
    )


def scatter_sum(value, axes, size):
    pieces = lax.all_to_all(value, axes, 0, 0, tiled=True)
    return jnp.sum(pieces.reshape((size, value.shape[0] // size) + value.shape[1:]), axis=0)


def on_device(
    sources,
    unite_weight,
    norm_gain,
    head_weight,
    doc_lengths,
    target_ids,
    teacher_ids,
    teacher_probs,
    sizes,
):
    tok_local = sources.shape[1]
    n_sm = sizes["segment"] * sizes["zlo"] * sizes["core"]

    n_zhi, n_y = sizes["zhi"], sizes["y"]
    own = sources[0]
    own_y = spread_gather(own, "y", n_y).reshape(n_y, 1, tok_local, -1)
    zhi_all = lax.all_gather(own, "zhi", axis=0, tiled=True).reshape(n_zhi, tok_local, -1)
    me = lax.axis_index("zhi")
    others = lax.dynamic_slice_in_dim(
        jnp.concatenate([zhi_all, zhi_all], axis=0), me + 1, n_zhi - 1, axis=0
    )
    others_y = spread_gather(others.reshape((n_zhi - 1) * tok_local, -1), "y", n_y)
    rotated = jnp.concatenate(
        [own_y, others_y.reshape(n_y, n_zhi - 1, tok_local, -1)], axis=1
    )
    tokens = n_y * n_zhi * tok_local
    part = jnp.dot(
        rotated.reshape(tokens, -1), unite_weight[0], preferred_element_type=jnp.float32
    ).astype(jnp.bfloat16)
    part = part.reshape(n_y, n_zhi, tok_local, -1)
    product = lax.dynamic_slice_in_dim(
        jnp.concatenate([part, part], axis=1), (n_zhi - me) % n_zhi, n_zhi, axis=1
    ).reshape(tokens, -1)
    product = lax.optimization_barrier(product)

    n_sc = sizes["segment"] * sizes["core"]
    pieces = lax.all_to_all(product, ("segment", "core"), 0, 0, tiled=True)
    chunk = tokens // n_sc
    united = jnp.sum(pieces.reshape(n_sc, chunk, -1).astype(jnp.float32), axis=0)
    united = scatter_sum(united, "zlo", sizes["zlo"])

    squares = jnp.sum(united * united, axis=1)
    n_seq = sizes["y"] * sizes["zhi"]
    squares = jnp.sum(spread_gather(squares[None], SEQ, n_seq), axis=0)
    hidden_part = (
        united * lax.rsqrt(squares / D + norm_eps)[:, None] * norm_gain[None, :]
    ).astype(jnp.bfloat16)
    hidden_chunk = lax.all_gather(hidden_part, "zlo", axis=0, tiled=True)
    spread = jnp.broadcast_to(hidden_chunk[None], (n_sc,) + hidden_chunk.shape)
    hidden = lax.all_to_all(
        spread.reshape(tokens, -1), ("segment", "core"), 0, 0, tiled=True
    )

    logits = jnp.dot(hidden, head_weight, preferred_element_type=jnp.float32)
    logits = scatter_sum(logits, "y", sizes["y"])
    logits = scatter_sum(logits, "zhi", sizes["zhi"])

    seq_index = lax.axis_index("y") * sizes["zhi"] + lax.axis_index("zhi")
    positions = seq_index * tok_local + jnp.arange(tok_local, dtype=jnp.int32)
    vocab_width = head_weight.shape[1]
    offset = lax.axis_index(SM) * vocab_width
    columns = offset + jnp.arange(vocab_width, dtype=jnp.int32)
    target_weight = (target_ids[:, None] == columns[None, :]).astype(jnp.float32)
    for top_slot in range(teacher_ids.shape[1]):
        hits = (teacher_ids[:, top_slot : top_slot + 1] == columns[None, :]).astype(
            jnp.float32
        )
        target_weight = target_weight + teacher_probs[:, top_slot : top_slot + 1] * hits

    row_peak = jnp.max(logits, axis=1)
    stats = jnp.stack(
        [
            row_peak,
            jnp.sum(jnp.exp(logits - row_peak[:, None]), axis=1),
            jnp.sum(target_weight * logits, axis=1),
        ]
    )
    n_sm = sizes["segment"] * sizes["zlo"] * sizes["core"]
    every = spread_gather(stats[None], SM, n_sm)
    peak = jnp.max(every[:, 0], axis=0)
    total = jnp.sum(every[:, 1] * jnp.exp(every[:, 0] - peak[None]), axis=0)
    lse = peak + jnp.log(total)
    picked = jnp.sum(every[:, 2], axis=0)

    target_mass = 1.0 + jnp.sum(teacher_probs, axis=1)
    doc_ends = jnp.cumsum(doc_lengths)
    is_last = jnp.any(positions[:, None] + 1 == doc_ends[None, :], axis=1)
    in_vocab = (target_ids < VOCAB).astype(jnp.float32)
    valid_rows = jnp.where(is_last, 0.0, in_vocab)
    per_token = valid_rows * (target_mass * lse - picked)
    loss_hi = per_token.astype(jnp.bfloat16)
    loss_lo = (per_token - loss_hi.astype(jnp.float32)).astype(jnp.bfloat16)

    logit_grad = (
        valid_rows[:, None]
        * (target_mass[:, None] * jnp.exp(logits - lse[:, None]) - target_weight)
    ).astype(jnp.bfloat16)
    extra = jnp.stack(
        [loss_hi, loss_lo, valid_rows.astype(jnp.bfloat16), jnp.zeros_like(loss_hi)],
        axis=1,
    )
    carried = jnp.concatenate([logit_grad, extra], axis=1)
    carried = lax.all_gather(carried, "zhi", axis=0, tiled=True)
    carried = spread_gather(carried, "y", sizes["y"])

    loss_sum = jnp.sum(
        carried[:, vocab_width].astype(jnp.float32)
        + carried[:, vocab_width + 1].astype(jnp.float32)
    )
    count = jnp.sum(carried[:, vocab_width + 2].astype(jnp.float32))
    mean_loss = loss_sum / jnp.maximum(count, 1.0)

    head_grad = lax.dot_general(
        hidden,
        carried[:, :vocab_width],
        (((0,), (0,)), ((), ())),
        preferred_element_type=jnp.float32,
    )
    return (mean_loss, head_grad)


def solution(mesh):
    n_seg, n_seq, n_mp = (mesh.shape[a] for a in ("segment", "seq", "mp"))
    sizes = {"segment": n_seg, "y": n_seq // 4, "zhi": 4, "zlo": n_mp // 2, "core": 2}
    fine = Mesh(
        mesh.devices.reshape(n_seg, sizes["y"], sizes["zhi"], sizes["zlo"], sizes["core"]),
        ("segment", "y", "zhi", "zlo", "core"),
    )
    placed = (
        P("segment", SEQ, ("zlo", "core")),
        P("segment", ("zlo", "core"), SEQ),
        P(SEQ),
        P(SEQ, SM),
        P(),
        P(SEQ),
        P(SEQ, None),
        P(SEQ, None),
    )

    def body(*args):
        return on_device(*args, sizes=sizes)

    return jax.shard_map(
        body,
        mesh=fine,
        in_specs=placed,
        out_specs=(P(), P(SEQ, SM)),
        check_vma=False,
    )
```

```python
import jax
import jax.numpy as jnp
from jax import lax
from jax.sharding import Mesh
from jax.sharding import PartitionSpec as P

D = 7168
VOCAB = 16000

norm_eps = 1e-06

SEQ = ("y", "zhi")
SM = ("segment", "zlo", "core")


def spread_gather(value, axes, size):
    spread = jnp.broadcast_to(value[None], (size,) + value.shape)
    return lax.all_to_all(
        spread.reshape((size * value.shape[0],) + value.shape[1:]), axes, 0, 0, tiled=True
    )


def scatter_sum(value, axes, size):
    pieces = lax.all_to_all(value, axes, 0, 0, tiled=True)
    return jnp.sum(pieces.reshape((size, value.shape[0] // size) + value.shape[1:]), axis=0)


def on_device(
    sources,
    unite_weight,
    norm_gain,
    head_weight,
    doc_lengths,
    target_ids,
    teacher_ids,
    teacher_probs,
    sizes,
):
    tok_local = sources.shape[1]
    n_sm = sizes["segment"] * sizes["zlo"] * sizes["core"]

    rows = lax.all_gather(sources[0], "zhi", axis=0, tiled=True)
    rows = spread_gather(rows, "y", sizes["y"])
    tokens = rows.shape[0]
    product = jnp.dot(rows, unite_weight[0], preferred_element_type=jnp.float32)
    product = lax.optimization_barrier(product.astype(jnp.bfloat16))

    n_sc = sizes["segment"] * sizes["core"]
    pieces = lax.all_to_all(product, ("segment", "core"), 0, 0, tiled=True)
    chunk = tokens // n_sc
    united = jnp.sum(pieces.reshape(n_sc, chunk, -1).astype(jnp.float32), axis=0)
    united = scatter_sum(united, "zlo", sizes["zlo"])

    squares = jnp.sum(united * united, axis=1)
    n_seq = sizes["y"] * sizes["zhi"]
    squares = jnp.sum(spread_gather(squares[None], SEQ, n_seq), axis=0)
    hidden_part = (
        united * lax.rsqrt(squares / D + norm_eps)[:, None] * norm_gain[None, :]
    ).astype(jnp.bfloat16)
    hidden_chunk = lax.all_gather(hidden_part, "zlo", axis=0, tiled=True)
    spread = jnp.broadcast_to(hidden_chunk[None], (n_sc,) + hidden_chunk.shape)
    hidden3 = lax.all_to_all(spread, ("segment", "core"), 0, 0, tiled=False)
    hidden = hidden3.reshape(tokens, -1)

    logits = jnp.einsum(
        "cti,iv->ctv", hidden3, head_weight, preferred_element_type=jnp.float32
    ).reshape(tokens, -1)
    logits = scatter_sum(logits, "y", sizes["y"])
    logits = scatter_sum(logits, "zhi", sizes["zhi"])

    seq_index = lax.axis_index("y") * sizes["zhi"] + lax.axis_index("zhi")
    positions = seq_index * tok_local + jnp.arange(tok_local, dtype=jnp.int32)
    vocab_width = head_weight.shape[1]
    offset = lax.axis_index(SM) * vocab_width
    columns = offset + jnp.arange(vocab_width, dtype=jnp.int32)
    target_weight = (target_ids[:, None] == columns[None, :]).astype(jnp.float32)
    for top_slot in range(teacher_ids.shape[1]):
        hits = (teacher_ids[:, top_slot : top_slot + 1] == columns[None, :]).astype(
            jnp.float32
        )
        target_weight = target_weight + teacher_probs[:, top_slot : top_slot + 1] * hits

    row_peak = jnp.max(logits, axis=1)
    stats = jnp.stack(
        [
            row_peak,
            jnp.sum(jnp.exp(logits - row_peak[:, None]), axis=1),
            jnp.sum(target_weight * logits, axis=1),
        ]
    )
    n_sm = sizes["segment"] * sizes["zlo"] * sizes["core"]
    every = spread_gather(stats[None], SM, n_sm)
    peak = jnp.max(every[:, 0], axis=0)
    total = jnp.sum(every[:, 1] * jnp.exp(every[:, 0] - peak[None]), axis=0)
    lse = peak + jnp.log(total)
    picked = jnp.sum(every[:, 2], axis=0)

    target_mass = 1.0 + jnp.sum(teacher_probs, axis=1)
    doc_ends = jnp.cumsum(doc_lengths)
    is_last = jnp.any(positions[:, None] + 1 == doc_ends[None, :], axis=1)
    in_vocab = (target_ids < VOCAB).astype(jnp.float32)
    valid_rows = jnp.where(is_last, 0.0, in_vocab)
    per_token = valid_rows * (target_mass * lse - picked)
    loss_hi = per_token.astype(jnp.bfloat16)
    loss_lo = (per_token - loss_hi.astype(jnp.float32)).astype(jnp.bfloat16)

    logit_grad = (
        valid_rows[:, None]
        * (target_mass[:, None] * jnp.exp(logits - lse[:, None]) - target_weight)
    ).astype(jnp.bfloat16)
    extra = jnp.stack(
        [loss_hi, loss_lo, valid_rows.astype(jnp.bfloat16), jnp.zeros_like(loss_hi)],
        axis=1,
    )
    carried = jnp.concatenate([logit_grad, extra], axis=1)
    carried = lax.all_gather(carried, "zhi", axis=0, tiled=True)
    carried = spread_gather(carried, "y", sizes["y"])

    loss_sum = jnp.sum(
        carried[:, vocab_width].astype(jnp.float32)
        + carried[:, vocab_width + 1].astype(jnp.float32)
    )
    count = jnp.sum(carried[:, vocab_width + 2].astype(jnp.float32))
    mean_loss = loss_sum / jnp.maximum(count, 1.0)

    head_grad = lax.dot_general(
        hidden,
        carried[:, :vocab_width],
        (((0,), (0,)), ((), ())),
        preferred_element_type=jnp.float32,
    )
    return (mean_loss, head_grad)


def solution(mesh):
    n_seg, n_seq, n_mp = (mesh.shape[a] for a in ("segment", "seq", "mp"))
    sizes = {"segment": n_seg, "y": n_seq // 4, "zhi": 4, "zlo": n_mp // 2, "core": 2}
    fine = Mesh(
        mesh.devices.reshape(n_seg, sizes["y"], sizes["zhi"], sizes["zlo"], sizes["core"]),
        ("segment", "y", "zhi", "zlo", "core"),
    )
    placed = (
        P("segment", SEQ, ("zlo", "core")),
        P("segment", ("zlo", "core"), SEQ),
        P(SEQ),
        P(SEQ, SM),
        P(),
        P(SEQ),
        P(SEQ, None),
        P(SEQ, None),
    )

    def body(*args):
        return on_device(*args, sizes=sizes)

    return jax.shard_map(
        body,
        mesh=fine,
        in_specs=placed,
        out_specs=(P(), P(SEQ, SM)),
        check_vma=False,
    )
```

```python
import jax
import jax.numpy as jnp
from jax import lax
from jax.sharding import Mesh
from jax.sharding import PartitionSpec as P

D = 7168
VOCAB = 16000

norm_eps = 1e-06

SEQ = ("y", "zhi")
SM = ("segment", "zlo", "core")


def spread_gather(value, axes, size):
    spread = jnp.broadcast_to(value[None], (size,) + value.shape)
    return lax.all_to_all(
        spread.reshape((size * value.shape[0],) + value.shape[1:]), axes, 0, 0, tiled=True
    )


def scatter_sum(value, axes, size):
    pieces = lax.all_to_all(value, axes, 0, 0, tiled=True)
    return jnp.sum(pieces.reshape((size, value.shape[0] // size) + value.shape[1:]), axis=0)


def on_device(
    sources,
    unite_weight,
    norm_gain,
    head_weight,
    doc_lengths,
    target_ids,
    teacher_ids,
    teacher_probs,
    sizes,
):
    tok_local = sources.shape[1]
    n_sm = sizes["segment"] * sizes["zlo"] * sizes["core"]

    rows = lax.all_gather(sources[0], "zhi", axis=0, tiled=True)
    rows = spread_gather(rows, "y", sizes["y"])
    tokens = rows.shape[0]
    product = jnp.dot(rows, unite_weight[0], preferred_element_type=jnp.float32)
    product = lax.optimization_barrier(product.astype(jnp.bfloat16))

    n_sc = sizes["segment"] * sizes["core"]
    pieces = lax.all_to_all(product, ("segment", "core"), 0, 0, tiled=True)
    chunk = tokens // n_sc
    united = jnp.sum(pieces.reshape(n_sc, chunk, -1).astype(jnp.float32), axis=0)
    united = scatter_sum(united, "zlo", sizes["zlo"])

    squares = jnp.sum(united * united, axis=1)
    n_seq = sizes["y"] * sizes["zhi"]
    squares = jnp.sum(spread_gather(squares[None], SEQ, n_seq), axis=0)
    hidden_part = (
        united * lax.rsqrt(squares / D + norm_eps)[:, None] * norm_gain[None, :]
    ).astype(jnp.bfloat16)
    hidden_chunk = lax.all_gather(hidden_part, "zlo", axis=0, tiled=True)
    spread = jnp.broadcast_to(hidden_chunk[None], (n_sc,) + hidden_chunk.shape)
    hidden = lax.all_to_all(
        spread.reshape(tokens, -1), ("segment", "core"), 0, 0, tiled=True
    )

    logits = jnp.dot(hidden, head_weight, preferred_element_type=jnp.float32)
    logits = scatter_sum(logits, "y", sizes["y"])
    logits = scatter_sum(logits, "zhi", sizes["zhi"])

    seq_index = lax.axis_index("y") * sizes["zhi"] + lax.axis_index("zhi")
    positions = seq_index * tok_local + jnp.arange(tok_local, dtype=jnp.int32)
    vocab_width = head_weight.shape[1]
    offset = lax.axis_index(SM) * vocab_width
    columns = offset + jnp.arange(vocab_width, dtype=jnp.int32)
    target_weight = (target_ids[:, None] == columns[None, :]).astype(jnp.float32)
    for top_slot in range(teacher_ids.shape[1]):
        hits = (teacher_ids[:, top_slot : top_slot + 1] == columns[None, :]).astype(
            jnp.float32
        )
        target_weight = target_weight + teacher_probs[:, top_slot : top_slot + 1] * hits

    row_peak = jnp.max(logits, axis=1)
    stats = jnp.stack(
        [
            row_peak,
            jnp.sum(jnp.exp(logits - row_peak[:, None]), axis=1),
            jnp.sum(target_weight * logits, axis=1),
        ]
    )
    n_sm = sizes["segment"] * sizes["zlo"] * sizes["core"]
    every = spread_gather(stats[None], SM, n_sm)
    peak = jnp.max(every[:, 0], axis=0)
    total = jnp.sum(every[:, 1] * jnp.exp(every[:, 0] - peak[None]), axis=0)
    lse = peak + jnp.log(total)
    picked = jnp.sum(every[:, 2], axis=0)

    target_mass = 1.0 + jnp.sum(teacher_probs, axis=1)
    doc_ends = jnp.cumsum(doc_lengths)
    is_last = jnp.any(positions[:, None] + 1 == doc_ends[None, :], axis=1)
    in_vocab = (target_ids < VOCAB).astype(jnp.float32)
    valid_rows = jnp.where(is_last, 0.0, in_vocab)
    per_token = valid_rows * (target_mass * lse - picked)
    loss_hi = per_token.astype(jnp.bfloat16)
    loss_lo = (per_token - loss_hi.astype(jnp.float32)).astype(jnp.bfloat16)

    logit_grad = (
        valid_rows[:, None]
        * (target_mass[:, None] * jnp.exp(logits - lse[:, None]) - target_weight)
    ).astype(jnp.bfloat16)
    extra = jnp.stack(
        [loss_hi, loss_lo, valid_rows.astype(jnp.bfloat16), jnp.zeros_like(loss_hi)],
        axis=1,
    )
    carried = jnp.concatenate([logit_grad, extra], axis=1)
    n_y, n_zhi = sizes["y"], sizes["zhi"]
    me = lax.axis_index("zhi")
    own_y = spread_gather(carried, "y", n_y).reshape(n_y, 1, tok_local, -1)
    zhi_all = lax.all_gather(carried, "zhi", axis=0, tiled=True).reshape(n_zhi, tok_local, -1)
    others = lax.dynamic_slice_in_dim(
        jnp.concatenate([zhi_all, zhi_all], axis=0), me + 1, n_zhi - 1, axis=0
    )
    others_y = spread_gather(others.reshape((n_zhi - 1) * tok_local, -1), "y", n_y)
    others_y = others_y.reshape(n_y, n_zhi - 1, tok_local, -1)

    rotated_extra = jnp.concatenate(
        [own_y[..., vocab_width:], others_y[..., vocab_width:]], axis=1
    )
    extra_all = lax.dynamic_slice_in_dim(
        jnp.concatenate([rotated_extra, rotated_extra], axis=1), (n_zhi - me) % n_zhi, n_zhi, axis=1
    ).reshape(-1, extra.shape[1]).astype(jnp.float32)
    loss_sum = jnp.sum(extra_all[:, 0] + extra_all[:, 1])
    count = jnp.sum(extra_all[:, 2])
    mean_loss = loss_sum / jnp.maximum(count, 1.0)

    hidden4 = hidden.reshape(n_y, n_zhi, tok_local, -1)
    hidden_own = lax.dynamic_slice_in_dim(hidden4, me, 1, axis=1)
    hidden_others = lax.dynamic_slice_in_dim(
        jnp.concatenate([hidden4, hidden4], axis=1), me + 1, n_zhi - 1, axis=1
    )
    head_grad = lax.dot_general(
        hidden_own.reshape(-1, hidden.shape[1]),
        own_y[..., :vocab_width].reshape(-1, vocab_width),
        (((0,), (0,)), ((), ())),
        preferred_element_type=jnp.float32,
    ) + lax.dot_general(
        hidden_others.reshape(-1, hidden.shape[1]),
        others_y[..., :vocab_width].reshape(-1, vocab_width),
        (((0,), (0,)), ((), ())),
        preferred_element_type=jnp.float32,
    )
    return (mean_loss, head_grad)


def solution(mesh):
    n_seg, n_seq, n_mp = (mesh.shape[a] for a in ("segment", "seq", "mp"))
    sizes = {"segment": n_seg, "y": n_seq // 4, "zhi": 4, "zlo": n_mp // 2, "core": 2}
    fine = Mesh(
        mesh.devices.reshape(n_seg, sizes["y"], sizes["zhi"], sizes["zlo"], sizes["core"]),
        ("segment", "y", "zhi", "zlo", "core"),
    )
    placed = (
        P("segment", SEQ, ("zlo", "core")),
        P("segment", ("zlo", "core"), SEQ),
        P(SEQ),
        P(SEQ, SM),
        P(),
        P(SEQ),
        P(SEQ, None),
        P(SEQ, None),
    )

    def body(*args):
        return on_device(*args, sizes=sizes)

    return jax.shard_map(
        body,
        mesh=fine,
        in_specs=placed,
        out_specs=(P(), P(SEQ, SM)),
        check_vma=False,
    )
```

```python
import jax
import jax.numpy as jnp
from jax import lax
from jax.sharding import Mesh
from jax.sharding import PartitionSpec as P

D = 7168
VOCAB = 16000

norm_eps = 1e-06

SEQ = ("y", "zhi")
SM = ("segment", "zlo", "core")


def spread_gather(value, axes, size):
    spread = jnp.broadcast_to(value[None], (size,) + value.shape)
    return lax.all_to_all(
        spread.reshape((size * value.shape[0],) + value.shape[1:]), axes, 0, 0, tiled=True
    )


def scatter_sum(value, axes, size):
    pieces = lax.all_to_all(value, axes, 0, 0, tiled=True)
    return jnp.sum(pieces.reshape((size, value.shape[0] // size) + value.shape[1:]), axis=0)


def on_device(
    sources,
    unite_weight,
    norm_gain,
    head_weight,
    doc_lengths,
    target_ids,
    teacher_ids,
    teacher_probs,
    sizes,
):
    tok_local = sources.shape[1]
    n_sm = sizes["segment"] * sizes["zlo"] * sizes["core"]

    n_y, n_zhi = sizes["y"], sizes["zhi"]
    me = lax.axis_index("zhi")
    own = sources[0]
    own_y = spread_gather(own, "y", n_y).reshape(n_y, 1, tok_local, -1)
    zhi_all = lax.all_gather(own, "zhi", axis=0, tiled=True).reshape(n_zhi, tok_local, -1)
    others = lax.dynamic_slice_in_dim(
        jnp.concatenate([zhi_all, zhi_all], axis=0), me + 1, n_zhi - 1, axis=0
    )
    others_y = spread_gather(others.reshape((n_zhi - 1) * tok_local, -1), "y", n_y)
    others_y = others_y.reshape(n_y, n_zhi - 1, tok_local, -1)
    rows = jnp.zeros((n_y, n_zhi, tok_local, own.shape[1]), own.dtype)
    rows = lax.dynamic_update_slice_in_dim(rows, own_y, me, axis=1)
    for k in range(n_zhi - 1):
        rows = lax.dynamic_update_slice_in_dim(
            rows, others_y[:, k : k + 1], (me + 1 + k) % n_zhi, axis=1
        )
    rows = rows.reshape(n_y * n_zhi * tok_local, -1)
    tokens = rows.shape[0]
    product = jnp.dot(rows, unite_weight[0], preferred_element_type=jnp.float32)
    product = lax.optimization_barrier(product.astype(jnp.bfloat16))

    n_sc = sizes["segment"] * sizes["core"]
    pieces = lax.all_to_all(product, ("segment", "core"), 0, 0, tiled=True)
    chunk = tokens // n_sc
    united = jnp.sum(pieces.reshape(n_sc, chunk, -1).astype(jnp.float32), axis=0)
    united = scatter_sum(united, "zlo", sizes["zlo"])

    squares = jnp.sum(united * united, axis=1)
    n_seq = sizes["y"] * sizes["zhi"]
    squares = jnp.sum(spread_gather(squares[None], SEQ, n_seq), axis=0)
    hidden_part = (
        united * lax.rsqrt(squares / D + norm_eps)[:, None] * norm_gain[None, :]
    ).astype(jnp.bfloat16)
    hidden_chunk = lax.all_gather(hidden_part, "zlo", axis=0, tiled=True)
    spread = jnp.broadcast_to(hidden_chunk[None], (n_sc,) + hidden_chunk.shape)
    hidden = lax.all_to_all(
        spread.reshape(tokens, -1), ("segment", "core"), 0, 0, tiled=True
    )

    logits = jnp.dot(hidden, head_weight, preferred_element_type=jnp.float32)
    logits = scatter_sum(logits, "y", sizes["y"])
    logits = scatter_sum(logits, "zhi", sizes["zhi"])

    seq_index = lax.axis_index("y") * sizes["zhi"] + lax.axis_index("zhi")
    positions = seq_index * tok_local + jnp.arange(tok_local, dtype=jnp.int32)
    vocab_width = head_weight.shape[1]
    offset = lax.axis_index(SM) * vocab_width
    columns = offset + jnp.arange(vocab_width, dtype=jnp.int32)
    target_weight = (target_ids[:, None] == columns[None, :]).astype(jnp.float32)
    for top_slot in range(teacher_ids.shape[1]):
        hits = (teacher_ids[:, top_slot : top_slot + 1] == columns[None, :]).astype(
            jnp.float32
        )
        target_weight = target_weight + teacher_probs[:, top_slot : top_slot + 1] * hits

    row_peak = jnp.max(logits, axis=1)
    stats = jnp.stack(
        [
            row_peak,
            jnp.sum(jnp.exp(logits - row_peak[:, None]), axis=1),
            jnp.sum(target_weight * logits, axis=1),
        ]
    )
    n_sm = sizes["segment"] * sizes["zlo"] * sizes["core"]
    every = spread_gather(stats[None], SM, n_sm)
    peak = jnp.max(every[:, 0], axis=0)
    total = jnp.sum(every[:, 1] * jnp.exp(every[:, 0] - peak[None]), axis=0)
    lse = peak + jnp.log(total)
    picked = jnp.sum(every[:, 2], axis=0)

    target_mass = 1.0 + jnp.sum(teacher_probs, axis=1)
    doc_ends = jnp.cumsum(doc_lengths)
    is_last = jnp.any(positions[:, None] + 1 == doc_ends[None, :], axis=1)
    in_vocab = (target_ids < VOCAB).astype(jnp.float32)
    valid_rows = jnp.where(is_last, 0.0, in_vocab)
    per_token = valid_rows * (target_mass * lse - picked)
    loss_hi = per_token.astype(jnp.bfloat16)
    loss_lo = (per_token - loss_hi.astype(jnp.float32)).astype(jnp.bfloat16)

    logit_grad = (
        valid_rows[:, None]
        * (target_mass[:, None] * jnp.exp(logits - lse[:, None]) - target_weight)
    ).astype(jnp.bfloat16)
    extra = jnp.stack(
        [loss_hi, loss_lo, valid_rows.astype(jnp.bfloat16), jnp.zeros_like(loss_hi)],
        axis=1,
    )
    carried = jnp.concatenate([logit_grad, extra], axis=1)
    own_y = spread_gather(carried, "y", n_y).reshape(n_y, 1, tok_local, -1)
    zhi_all = lax.all_gather(carried, "zhi", axis=0, tiled=True).reshape(n_zhi, tok_local, -1)
    others = lax.dynamic_slice_in_dim(
        jnp.concatenate([zhi_all, zhi_all], axis=0), me + 1, n_zhi - 1, axis=0
    )
    others_y = spread_gather(others.reshape((n_zhi - 1) * tok_local, -1), "y", n_y)
    others_y = others_y.reshape(n_y, n_zhi - 1, tok_local, -1)

    rotated_extra = jnp.concatenate(
        [own_y[..., vocab_width:], others_y[..., vocab_width:]], axis=1
    )
    extra_all = lax.dynamic_slice_in_dim(
        jnp.concatenate([rotated_extra, rotated_extra], axis=1), (n_zhi - me) % n_zhi, n_zhi, axis=1
    ).reshape(-1, extra.shape[1]).astype(jnp.float32)
    loss_sum = jnp.sum(extra_all[:, 0] + extra_all[:, 1])
    count = jnp.sum(extra_all[:, 2])
    mean_loss = loss_sum / jnp.maximum(count, 1.0)

    hidden4 = hidden.reshape(n_y, n_zhi, tok_local, -1)
    hidden_own = lax.dynamic_slice_in_dim(hidden4, me, 1, axis=1)
    hidden_others = lax.dynamic_slice_in_dim(
        jnp.concatenate([hidden4, hidden4], axis=1), me + 1, n_zhi - 1, axis=1
    )
    head_grad = lax.dot_general(
        hidden_own.reshape(-1, hidden.shape[1]),
        own_y[..., :vocab_width].reshape(-1, vocab_width),
        (((0,), (0,)), ((), ())),
        preferred_element_type=jnp.float32,
    ) + lax.dot_general(
        hidden_others.reshape(-1, hidden.shape[1]),
        others_y[..., :vocab_width].reshape(-1, vocab_width),
        (((0,), (0,)), ((), ())),
        preferred_element_type=jnp.float32,
    )
    return (mean_loss, head_grad)


def solution(mesh):
    n_seg, n_seq, n_mp = (mesh.shape[a] for a in ("segment", "seq", "mp"))
    sizes = {"segment": n_seg, "y": n_seq // 4, "zhi": 4, "zlo": n_mp // 2, "core": 2}
    fine = Mesh(
        mesh.devices.reshape(n_seg, sizes["y"], sizes["zhi"], sizes["zlo"], sizes["core"]),
        ("segment", "y", "zhi", "zlo", "core"),
    )
    placed = (
        P("segment", SEQ, ("zlo", "core")),
        P("segment", ("zlo", "core"), SEQ),
        P(SEQ),
        P(SEQ, SM),
        P(),
        P(SEQ),
        P(SEQ, None),
        P(SEQ, None),
    )

    def body(*args):
        return on_device(*args, sizes=sizes)

    return jax.shard_map(
        body,
        mesh=fine,
        in_specs=placed,
        out_specs=(P(), P(SEQ, SM)),
        check_vma=False,
    )
```

```python
import jax
import jax.numpy as jnp
from jax import lax
from jax.sharding import Mesh
from jax.sharding import PartitionSpec as P

D = 7168
VOCAB = 16000

norm_eps = 1e-06

SEQ = ("y", "zhi")
SM = ("segment", "zlo", "core")


def spread_gather(value, axes, size):
    spread = jnp.broadcast_to(value[None], (size,) + value.shape)
    return lax.all_to_all(
        spread.reshape((size * value.shape[0],) + value.shape[1:]), axes, 0, 0, tiled=True
    )


def scatter_sum(value, axes, size):
    pieces = lax.all_to_all(value, axes, 0, 0, tiled=True)
    return jnp.sum(pieces.reshape((size, value.shape[0] // size) + value.shape[1:]), axis=0)


def on_device(
    sources,
    unite_weight,
    norm_gain,
    head_weight,
    doc_lengths,
    target_ids,
    teacher_ids,
    teacher_probs,
    sizes,
):
    tok_local = sources.shape[1]
    n_sm = sizes["segment"] * sizes["zlo"] * sizes["core"]

    rows = lax.all_gather(sources[0], "zhi", axis=0, tiled=True)
    rows = spread_gather(rows, "y", sizes["y"])
    tokens = rows.shape[0]
    product = jnp.dot(rows, unite_weight[0], preferred_element_type=jnp.float32)
    product = lax.optimization_barrier(product.astype(jnp.bfloat16))

    n_sc = sizes["segment"] * sizes["core"]
    pieces = lax.all_to_all(product, ("segment", "core"), 0, 0, tiled=True)
    chunk = tokens // n_sc
    united = jnp.sum(pieces.reshape(n_sc, chunk, -1).astype(jnp.float32), axis=0)
    united = scatter_sum(united, "zlo", sizes["zlo"])

    n_seq = sizes["y"] * sizes["zhi"]
    squares = jnp.sum(united * united, axis=1)
    squares = spread_gather(squares[None], ("y", "zhi", "zlo"), n_seq * sizes["zlo"])
    squares = jnp.sum(squares.reshape(n_seq, sizes["zlo"] * squares.shape[-1]), axis=0)
    united_chunk = lax.all_gather(united, "zlo", axis=0, tiled=True)
    hidden_chunk = (
        united_chunk * lax.rsqrt(squares / D + norm_eps)[:, None] * norm_gain[None, :]
    ).astype(jnp.bfloat16)
    spread = jnp.broadcast_to(hidden_chunk[None], (n_sc,) + hidden_chunk.shape)
    hidden = lax.all_to_all(
        spread.reshape(tokens, -1), ("segment", "core"), 0, 0, tiled=True
    )

    logits = jnp.dot(hidden, head_weight, preferred_element_type=jnp.float32)
    logits = scatter_sum(logits, "y", sizes["y"])
    logits = scatter_sum(logits, "zhi", sizes["zhi"])

    seq_index = lax.axis_index("y") * sizes["zhi"] + lax.axis_index("zhi")
    positions = seq_index * tok_local + jnp.arange(tok_local, dtype=jnp.int32)
    vocab_width = head_weight.shape[1]
    offset = lax.axis_index(SM) * vocab_width
    columns = offset + jnp.arange(vocab_width, dtype=jnp.int32)
    target_weight = (target_ids[:, None] == columns[None, :]).astype(jnp.float32)
    for top_slot in range(teacher_ids.shape[1]):
        hits = (teacher_ids[:, top_slot : top_slot + 1] == columns[None, :]).astype(
            jnp.float32
        )
        target_weight = target_weight + teacher_probs[:, top_slot : top_slot + 1] * hits

    row_peak = jnp.max(logits, axis=1)
    stats = jnp.stack(
        [
            row_peak,
            jnp.sum(jnp.exp(logits - row_peak[:, None]), axis=1),
            jnp.sum(target_weight * logits, axis=1),
        ]
    )
    n_sm = sizes["segment"] * sizes["zlo"] * sizes["core"]
    every = spread_gather(stats[None], SM, n_sm)
    peak = jnp.max(every[:, 0], axis=0)
    total = jnp.sum(every[:, 1] * jnp.exp(every[:, 0] - peak[None]), axis=0)
    lse = peak + jnp.log(total)
    picked = jnp.sum(every[:, 2], axis=0)

    target_mass = 1.0 + jnp.sum(teacher_probs, axis=1)
    doc_ends = jnp.cumsum(doc_lengths)
    is_last = jnp.any(positions[:, None] + 1 == doc_ends[None, :], axis=1)
    in_vocab = (target_ids < VOCAB).astype(jnp.float32)
    valid_rows = jnp.where(is_last, 0.0, in_vocab)
    per_token = valid_rows * (target_mass * lse - picked)
    loss_hi = per_token.astype(jnp.bfloat16)
    loss_lo = (per_token - loss_hi.astype(jnp.float32)).astype(jnp.bfloat16)

    logit_grad = (
        valid_rows[:, None]
        * (target_mass[:, None] * jnp.exp(logits - lse[:, None]) - target_weight)
    ).astype(jnp.bfloat16)
    extra = jnp.stack(
        [loss_hi, loss_lo, valid_rows.astype(jnp.bfloat16), jnp.zeros_like(loss_hi)],
        axis=1,
    )
    carried = jnp.concatenate([logit_grad, extra], axis=1)
    n_y, n_zhi = sizes["y"], sizes["zhi"]
    me = lax.axis_index("zhi")
    own_y = spread_gather(carried, "y", n_y).reshape(n_y, 1, tok_local, -1)
    zhi_all = lax.all_gather(carried, "zhi", axis=0, tiled=True).reshape(n_zhi, tok_local, -1)
    others = lax.dynamic_slice_in_dim(
        jnp.concatenate([zhi_all, zhi_all], axis=0), me + 1, n_zhi - 1, axis=0
    )
    others_y = spread_gather(others.reshape((n_zhi - 1) * tok_local, -1), "y", n_y)
    others_y = others_y.reshape(n_y, n_zhi - 1, tok_local, -1)

    rotated_extra = jnp.concatenate(
        [own_y[..., vocab_width:], others_y[..., vocab_width:]], axis=1
    )
    extra_all = lax.dynamic_slice_in_dim(
        jnp.concatenate([rotated_extra, rotated_extra], axis=1), (n_zhi - me) % n_zhi, n_zhi, axis=1
    ).reshape(-1, extra.shape[1]).astype(jnp.float32)
    loss_sum = jnp.sum(extra_all[:, 0] + extra_all[:, 1])
    count = jnp.sum(extra_all[:, 2])
    mean_loss = loss_sum / jnp.maximum(count, 1.0)

    hidden4 = hidden.reshape(n_y, n_zhi, tok_local, -1)
    hidden_own = lax.dynamic_slice_in_dim(hidden4, me, 1, axis=1)
    hidden_others = lax.dynamic_slice_in_dim(
        jnp.concatenate([hidden4, hidden4], axis=1), me + 1, n_zhi - 1, axis=1
    )
    head_grad = lax.dot_general(
        hidden_own.reshape(-1, hidden.shape[1]),
        own_y[..., :vocab_width].reshape(-1, vocab_width),
        (((0,), (0,)), ((), ())),
        preferred_element_type=jnp.float32,
    ) + lax.dot_general(
        hidden_others.reshape(-1, hidden.shape[1]),
        others_y[..., :vocab_width].reshape(-1, vocab_width),
        (((0,), (0,)), ((), ())),
        preferred_element_type=jnp.float32,
    )
    return (mean_loss, head_grad)


def solution(mesh):
    n_seg, n_seq, n_mp = (mesh.shape[a] for a in ("segment", "seq", "mp"))
    sizes = {"segment": n_seg, "y": n_seq // 4, "zhi": 4, "zlo": n_mp // 2, "core": 2}
    fine = Mesh(
        mesh.devices.reshape(n_seg, sizes["y"], sizes["zhi"], sizes["zlo"], sizes["core"]),
        ("segment", "y", "zhi", "zlo", "core"),
    )
    placed = (
        P("segment", SEQ, ("zlo", "core")),
        P("segment", ("zlo", "core"), SEQ),
        P(SEQ),
        P(SEQ, SM),
        P(),
        P(SEQ),
        P(SEQ, None),
        P(SEQ, None),
    )

    def body(*args):
        return on_device(*args, sizes=sizes)

    return jax.shard_map(
        body,
        mesh=fine,
        in_specs=placed,
        out_specs=(P(), P(SEQ, SM)),
        check_vma=False,
    )
```
